32 devices in a mesh: outer: 4 (over y, core), inner: 8 (over z, x).
Axes of the slice: x: 2, y: 2, z: 4, core: 2. Of those that a mesh axis runs over, the one named last changes fastest.
Arguments:
- token_ids: int32 [32768], P(('outer', 'inner')), may hold values from 0 to 50303, as said below
- inner_x: bfloat16 [32768, 512], P(('outer', 'inner')), may hold values from -6 to 6
- out_gate: bfloat16 [32768, 512], P(('outer', 'inner')), may hold values from -6 to 6
- gate_pre: float32 [2, 32768], P(None, ('outer', 'inner')), may hold values from -4 to 300
- conv_weight: float32 [4, 512], replicated, may hold values from -3 to 3
- qkv_weight: bfloat16 [3, 4, 4, 128], replicated, may hold values from -3 to 3
- norm_gain: float32 [512], replicated, may hold values from 0.1 to 1.9
- skip_gain: float32 [512], replicated, may hold values from 0.1 to 1.9
Outputs:
- gated_out: bfloat16 [32768, 512], P(('outer', 'inner'))
The draws below stay inside these ranges and needn't reach their ends.
Inputs may be any that keep to these rules, and one draw needn't show every extreme that they name: `token_ids`: A token with id 0 is a document delimiter: it starts a new document, and no earlier token reaches it or any later token.
All inputs are finite; a program needn't handle non-finite values.
Results may differ from the reference program's by a relative error of at most 0.012.
The reference program's roundings to bfloat16 on the way count: a program that leaves them out, or rounds other values in their place, can miss the bound.
Values may be sent and summed in bfloat16 or wider, within the bound.
No kernel may reach another device: no remote copies, remote signals or barrier semaphores. Data moves between devices by JAX's collectives and lax.ppermute only.
A program may use at most 64 MiB of HBM per device.

```python
import math
import jax
import jax.numpy as jnp
from jax import lax

DH = 512
KS = 4
BS = 4
VOCAB = 50304
TOK_DEV = 1024
STREAM_TOKENS = 32768


def draw_token_ids(key, part):
    key_words = jax.random.fold_in(key, 11)
    key_breaks = jax.random.fold_in(key, 12)
    key_places = jax.random.fold_in(key, 13)
    words = jax.random.randint(key_words, (STREAM_TOKENS,), 1, VOCAB)
    breaks = jax.random.randint(key_breaks, (STREAM_TOKENS,), 0, TOK_DEV * 64) == 0
    words = jnp.where(breaks, 0, words)
    places = jax.random.randint(key_places, (2,), 0, STREAM_TOKENS)
    token_position = jnp.arange(STREAM_TOKENS)
    words = jnp.where(token_position == places[0], VOCAB - 1, words)
    words = jnp.where(token_position == places[1], 0, words)
    return words.astype(jnp.int32)


def draw_gate_pre(key, part):
    token_position = jnp.arange(STREAM_TOKENS)
    key_input = jax.random.fold_in(key, 21)
    key_forget = jax.random.fold_in(key, 22)
    key_spurt_start = jax.random.fold_in(key, 23)
    key_spurt_length = jax.random.fold_in(key, 24)
    input_gate = jax.random.uniform(key_input, (STREAM_TOKENS,), jnp.float32, -4.0, 4.0)
    forget_base = math.log(STREAM_TOKENS / 0.7) + jax.random.uniform(key_forget, (STREAM_TOKENS,), jnp.float32, -1.0, 1.0)
    spurt_start = jax.random.randint(key_spurt_start, (3,), 0, STREAM_TOKENS)
    spurt_length = jax.random.uniform(key_spurt_length, (3,), jnp.float32, 0.0, 1.4)
    forget_gate_values = forget_base
    for token_index in range(3):
        forget_gate_values = jnp.where(token_position == spurt_start[token_index], spurt_length[token_index], forget_gate_values)
    return jnp.stack([input_gate, forget_gate_values], axis=0).astype(jnp.float32)


def steps_of(key, dims, cuts, smallest, high):
    loudness, own = 1.0, jax.random.fold_in(key, 6)
    for position, parts in cuts:
        draws = jnp.exp(jax.random.uniform(jax.random.fold_in(own, position), (parts,), jnp.float32, smallest / len(cuts), high / len(cuts)))
        loudness = loudness * jnp.repeat(draws, dims[position] // parts).reshape([-1 if axis == position else 1 for axis in range(len(dims))])
    return loudness


def scatter_about(own_key, shape, deviation, limit, split=(), held_as=jnp.bfloat16):
    gain = steps_of(own_key, shape, split, -0.22, 0.18) if split else 1.0
    values = jax.random.normal(own_key, shape, jnp.float32) * deviation * gain
    return jnp.minimum(jnp.maximum(values, -limit), limit).astype(held_as)


def setup_inputs(seed: int = 0) -> dict:
    keys = jax.random.split(jax.random.key(seed), 9)
    return {
        "token_ids": draw_token_ids(jax.random.fold_in(keys[8], 71), 0),
        "inner_x": scatter_about(keys[1], (STREAM_TOKENS, DH), 1.0, 6.0, ((0, 32),)),
        "out_gate": scatter_about(keys[2], (STREAM_TOKENS, DH), 1.0, 6.0, ((0, 32),)),
        "gate_pre": draw_gate_pre(jax.random.fold_in(keys[8], 71), 0),
        "conv_weight": scatter_about(keys[4], (KS, DH), KS ** -0.5, 3.0, (), jnp.float32),
        "qkv_weight": scatter_about(keys[5], (3, BS, BS, DH // BS), BS ** -0.5, 3.0),
        "norm_gain": jnp.clip(1.0 + 0.18 * jax.random.normal(keys[6], (DH,), jnp.float32), 0.1, 1.9),
        "skip_gain": jnp.clip(1.0 + 0.18 * jax.random.normal(keys[7], (DH,), jnp.float32), 0.1, 1.9),
    }


HIGHEST = lax.Precision.HIGHEST

def block_project(source, block_table):
    num_rows = source.shape[0]
    grouped = source.astype(jnp.float32).reshape(num_rows, DH // BS, BS)
    mapped = jnp.einsum('rbi,ijb->rbj', grouped, block_table.astype(jnp.float32), precision=HIGHEST)
    return mapped.reshape(num_rows, DH)

def reference(token_ids, inner_x, out_gate, gate_pre, conv_weight, qkv_weight, norm_gain, skip_gain):
    span_rows = 64
    span_count = STREAM_TOKENS // span_rows
    key_scale = DH ** (-0.5)
    sliced = (inner_x.reshape(span_count, span_rows, DH), out_gate.reshape(span_count, span_rows, DH), token_ids.reshape(span_count, span_rows), gate_pre[0].reshape(span_count, span_rows), gate_pre[1].reshape(span_count, span_rows))
    initial = (jnp.zeros((DH, DH), jnp.float32), jnp.array(-jnp.inf, dtype=jnp.float32), jnp.zeros((KS - 1, DH), inner_x.dtype))
    token_position = jnp.arange(span_rows)
    causal = token_position[None, :] <= token_position[:, None]

    def advance(running, pieces):
        memory, stabilizer, history = running
        input_span, gate_span, token_span, input_gate, forget_pre = pieces
        extended = jnp.concatenate([history, input_span], axis=0).astype(jnp.float32)
        conv_sum = jnp.zeros((span_rows, DH), jnp.float32)
        for offset in range(KS):
            conv_sum = conv_sum + conv_weight[offset] * extended[offset:offset + span_rows]
        convolved = jax.nn.silu(conv_sum).astype(jnp.bfloat16)
        query_rows = block_project(convolved, qkv_weight[0]).astype(jnp.bfloat16)
        key_rows = (block_project(convolved, qkv_weight[1]) * key_scale).astype(jnp.bfloat16)
        value_rows = block_project(input_span, qkv_weight[2]).astype(jnp.bfloat16)
        log_decay = jnp.cumsum(jax.nn.log_sigmoid(forget_pre))
        doc_marks = jnp.cumsum((token_span == 0).astype(jnp.int32))
        valid = causal & (doc_marks[None, :] == doc_marks[:, None])
        log_weight = jnp.where(valid, log_decay[:, None] - log_decay[None, :] + input_gate[None, :], -jnp.inf)
        carried = jnp.where(doc_marks == 0, log_decay + stabilizer, -jnp.inf)
        row_max = jnp.maximum(carried, lax.optimization_barrier(jnp.max(log_weight, axis=1)))
        scores = jnp.dot(query_rows, key_rows.T, preferred_element_type=jnp.float32)
        weights = jnp.exp(log_weight - row_max[:, None]) * scores
        value_float = value_rows.astype(jnp.float32)
        retrieved = jnp.exp(carried - row_max)[:, None] * jnp.dot(query_rows.astype(jnp.float32), memory, precision=HIGHEST)
        retrieved = retrieved + jnp.dot(weights, value_float, precision=HIGHEST)
        last_mark = doc_marks[span_rows - 1]
        tail_weight = jnp.where(doc_marks == last_mark, log_decay[span_rows - 1] - log_decay + input_gate, -jnp.inf)
        keep_weight = jnp.where(last_mark == 0, log_decay[span_rows - 1] + stabilizer, -jnp.inf)
        new_level = jnp.maximum(keep_weight, jnp.max(tail_weight))
        scaled_keys = jnp.exp(tail_weight - new_level)[:, None] * key_rows.astype(jnp.float32)
        new_memory = jnp.exp(keep_weight - new_level) * memory + jnp.dot(scaled_keys.T, value_float, precision=HIGHEST)
        average = lax.optimization_barrier(jnp.mean(retrieved, axis=1, keepdims=True))
        centered = retrieved - average
        variance = lax.optimization_barrier(jnp.mean(centered * centered, axis=1, keepdims=True))
        normed = centered * lax.rsqrt(variance + 1e-05) * norm_gain
        gated_rows = ((normed + skip_gain * convolved.astype(jnp.float32)) * jax.nn.silu(gate_span.astype(jnp.float32))).astype(jnp.bfloat16)
        new_history = input_span[span_rows - KS + 1:]
        return ((new_memory, new_level, new_history), gated_rows)
    final_state, outputs = lax.scan(advance, initial, sliced)
    return outputs.reshape(STREAM_TOKENS, DH)
```

```python
import jax
import jax.numpy as jnp
from jax import lax
from jax.sharding import PartitionSpec as P

HIGHEST = lax.Precision.HIGHEST
AXES = ("outer", "inner")
PAD_ROWS = 8


def passed_along(shard, axis, by):
    size = lax.axis_size(axis)
    pairs = [(i, i + by) for i in range(size) if 0 <= i + by < size]
    return lax.ppermute(shard, axis, pairs)


def dense_blocks(block_table, channels):
    group_size = block_table.shape[0]
    index_rows = jnp.arange(channels)
    same_block = index_rows[:, None] // group_size == index_rows[None, :] // group_size
    lane_phase = index_rows % group_size
    dense_matrix = jnp.zeros((channels, channels), jnp.float32)
    for column in range(group_size):
        column_values = block_table[:, column, :].T.reshape(channels).astype(jnp.float32)
        dense_matrix = dense_matrix + column_values[:, None] * (lane_phase[None, :] == column)
    return jnp.where(same_block, dense_matrix, 0.0).astype(block_table.dtype)


def combine(earlier, later):
    memory_first, level_first, decay_first, cut_first = earlier
    memory_second, level_second, decay_second, cut_second = later
    kept_level = jnp.where(cut_second > 0.5, -jnp.inf, level_first + decay_second)
    new_level = jnp.maximum(kept_level, level_second)
    safe_level = jnp.where(new_level == -jnp.inf, 0.0, new_level)
    new_memory = (
        jnp.exp(kept_level - safe_level) * memory_first
        + jnp.exp(level_second - safe_level) * memory_second
    )
    return (new_memory, new_level, decay_first + decay_second, jnp.maximum(cut_first, cut_second))


def pack(state):
    memory, level, decay, cut = state
    channels = memory.shape[1]
    lane = jnp.arange(channels)[None, :]
    row = jnp.where(lane == 0, level, jnp.where(lane == 1, decay, jnp.where(lane == 2, cut, 0.0)))
    extra = jnp.concatenate([row, jnp.zeros((PAD_ROWS - 1, channels), jnp.float32)], axis=0)
    return jnp.concatenate([memory, extra], axis=0)


def unpack(message, rows):
    return message[:rows], message[rows, 0], message[rows, 1], message[rows, 2]


def exclusive_prefix(own_state, me, count):
    rows = own_state[0].shape[0]
    inclusive = own_state
    exclusive = None
    distance = 1
    while distance < count:
        arrived = unpack(passed_along(pack(inclusive), AXES, distance), rows)
        present = me >= distance
        memory, level, decay, cut = arrived
        arrived = (
            memory,
            jnp.where(present, level, -jnp.inf),
            jnp.where(present, decay, 0.0),
            jnp.where(present, cut, 0.0),
        )
        exclusive = arrived if exclusive is None else combine(arrived, exclusive)
        if 2 * distance < count:
            inclusive = combine(arrived, inclusive)
        distance *= 2
    return exclusive


def body(token_ids, inner_x, out_gate, gate_pre, conv_weight, qkv_weight, norm_gain, skip_gain):
    num_rows, channels = inner_x.shape
    kernel_taps = conv_weight.shape[0]
    rim_rows = passed_along(inner_x[num_rows - kernel_taps + 1 :], AXES, 1)
    extended = jnp.concatenate([rim_rows, inner_x], axis=0)
    conv_sum = jnp.zeros((num_rows, channels), jnp.float32)
    for offset in range(kernel_taps):
        conv_sum = conv_sum + conv_weight[offset] * extended[offset : offset + num_rows].astype(
            jnp.float32
        )
    convolved = jax.nn.silu(conv_sum).astype(jnp.bfloat16)
    query_rows = jnp.dot(
        convolved, dense_blocks(qkv_weight[0], channels), preferred_element_type=jnp.float32
    ).astype(jnp.bfloat16)
    key_rows = (
        jnp.dot(
            convolved, dense_blocks(qkv_weight[1], channels), preferred_element_type=jnp.float32
        )
        * channels ** (-0.5)
    ).astype(jnp.bfloat16)
    value_rows = jnp.dot(
        inner_x, dense_blocks(qkv_weight[2], channels), preferred_element_type=jnp.float32
    ).astype(jnp.bfloat16)
    input_gate = gate_pre[0]
    log_decay = jnp.cumsum(jax.nn.log_sigmoid(gate_pre[1]))
    doc_marks = jnp.cumsum((token_ids == 0).astype(jnp.int32))
    last_mark = doc_marks[num_rows - 1]
    value_float = value_rows.astype(jnp.float32)
    tail_weight = jnp.where(
        doc_marks == last_mark, log_decay[num_rows - 1] - log_decay + input_gate, -jnp.inf
    )
    tail_level = jnp.max(tail_weight)
    weighted_keys = jnp.exp(tail_weight - tail_level)[:, None] * key_rows.astype(jnp.float32)
    summary = lax.dot_general(
        weighted_keys, value_float, (((0,), (0,)), ((), ())), precision=HIGHEST
    )
    own_state = (summary, tail_level, log_decay[num_rows - 1], (last_mark > 0).astype(jnp.float32))
    incoming = exclusive_prefix(own_state, lax.axis_index(AXES), lax.axis_size(AXES))
    token_position = jnp.arange(num_rows)
    valid = (token_position[None, :] <= token_position[:, None]) & (
        doc_marks[None, :] == doc_marks[:, None]
    )
    log_weight = jnp.where(
        valid, log_decay[:, None] - log_decay[None, :] + input_gate[None, :], -jnp.inf
    )
    local_max = jnp.max(log_weight, axis=1)
    scores = lax.dot_general(
        query_rows, key_rows, (((1,), (1,)), ((), ())), preferred_element_type=jnp.float32
    )
    weights = jnp.exp(log_weight - local_max[:, None]) * scores
    local_sum = jnp.dot(weights, value_float, precision=HIGHEST)
    carried = jnp.where(doc_marks == 0, log_decay + incoming[1], -jnp.inf)
    row_max = jnp.maximum(carried, local_max)
    from_memory = jnp.dot(query_rows.astype(jnp.float32), incoming[0], precision=HIGHEST)
    retrieved = (
        jnp.exp(carried - row_max)[:, None] * from_memory
        + jnp.exp(local_max - row_max)[:, None] * local_sum
    )
    average = jnp.mean(retrieved, axis=1, keepdims=True)
    centered = retrieved - average
    variance = jnp.mean(centered * centered, axis=1, keepdims=True)
    normed = centered * lax.rsqrt(variance + 1e-05) * norm_gain
    gated_rows = (normed + skip_gain * convolved.astype(jnp.float32)) * jax.nn.silu(
        out_gate.astype(jnp.float32)
    )
    return gated_rows.astype(jnp.bfloat16)


def solution(mesh):
    return jax.shard_map(
        body,
        mesh=mesh,
        in_specs=(
            P(AXES),
            P(AXES, None),
            P(AXES, None),
            P(None, AXES),
            P(),
            P(),
            P(),
            P(),
        ),
        out_specs=P(AXES, None),
        check_vma=False,
    )
```

```python
import jax
import jax.numpy as jnp
from jax import lax
from jax.sharding import PartitionSpec as P

HIGHEST = lax.Precision.HIGHEST
AXES = ("outer", "inner")
PAD_ROWS = 8
MESSAGE_DTYPE = jnp.float32


def passed_along(shard, axis, by):
    size = lax.axis_size(axis)
    pairs = [(i, i + by) for i in range(size) if 0 <= i + by < size]
    return lax.ppermute(shard, axis, pairs)


def dense_blocks(block_table, channels):
    group_size = block_table.shape[0]
    index_rows = jnp.arange(channels)
    same_block = index_rows[:, None] // group_size == index_rows[None, :] // group_size
    lane_phase = index_rows % group_size
    dense_matrix = jnp.zeros((channels, channels), jnp.float32)
    for column in range(group_size):
        column_values = block_table[:, column, :].T.reshape(channels).astype(jnp.float32)
        dense_matrix = dense_matrix + column_values[:, None] * (lane_phase[None, :] == column)
    return jnp.where(same_block, dense_matrix, 0.0).astype(block_table.dtype)


def split_bf16(values):
    high = lax.reduce_precision(values, exponent_bits=8, mantissa_bits=7)
    return high.astype(jnp.bfloat16), (values - high).astype(jnp.bfloat16)


def dot_two_pass(left, right, dims):
    high, low = split_bf16(left)
    first = lax.dot_general(high, right, dims, preferred_element_type=jnp.float32)
    return first + lax.dot_general(low, right, dims, preferred_element_type=jnp.float32)


def dot_any(left, right_message, dims):
    if right_message.dtype == jnp.bfloat16:
        return lax.dot_general(left, right_message, dims, preferred_element_type=jnp.float32)
    high, low = split_bf16(right_message)
    first = lax.dot_general(left, high, dims, preferred_element_type=jnp.float32)
    return first + lax.dot_general(left, low, dims, preferred_element_type=jnp.float32)


def combine(earlier, later):
    memory_first, level_first, decay_first, cut_first = earlier
    memory_second, level_second, decay_second, cut_second = later
    kept_level = jnp.where(cut_second > 0.5, -jnp.inf, level_first + decay_second)
    new_level = jnp.maximum(kept_level, level_second)
    safe_level = jnp.where(new_level == -jnp.inf, 0.0, new_level)
    new_memory = (
        jnp.exp(kept_level - safe_level) * memory_first
        + jnp.exp(level_second - safe_level) * memory_second
    )
    return (new_memory, new_level, decay_first + decay_second, jnp.maximum(cut_first, cut_second))


def pack(state):
    memory, level, decay, cut = state
    channels = memory.shape[1]
    lane = jnp.arange(channels)[None, :]
    scalars = [level, decay, cut]
    if MESSAGE_DTYPE == jnp.bfloat16:
        parts = []
        for value in scalars:
            high = lax.reduce_precision(value, exponent_bits=8, mantissa_bits=7)
            rest = value - high
            middle = lax.reduce_precision(rest, exponent_bits=8, mantissa_bits=7)
            parts.append((high, middle, rest - middle))
        rows = [
            sum(jnp.where(lane == index, parts[index][piece], 0.0) for index in range(3))
            for piece in range(3)
        ]
    else:
        rows = [sum(jnp.where(lane == index, scalars[index], 0.0) for index in range(3))]
    pad_rows = PAD_ROWS - len(rows)
    extra = jnp.concatenate(rows + [jnp.zeros((pad_rows, channels), jnp.float32)], axis=0)
    return jnp.concatenate([memory.astype(MESSAGE_DTYPE), extra.astype(MESSAGE_DTYPE)], axis=0)


def unpack(message, rows):
    if MESSAGE_DTYPE == jnp.bfloat16:
        tail = message[rows : rows + 3, :3].astype(jnp.float32)
        scalars = (tail[0] + tail[1]) + tail[2]
    else:
        scalars = message[rows, :3]
    return message[:rows], scalars[0], scalars[1], scalars[2]


def scan_and_read(own_state, me, count, query_rows, local_parts):
    rows = own_state[0].shape[0]
    inclusive = own_state
    earlier = None
    total = None
    distance = 1
    while distance < count:
        message = passed_along(pack(inclusive), AXES, distance)
        if earlier is None:
            message, local_parts = lax.optimization_barrier((message, local_parts))
        memory, level, decay, cut = unpack(message, rows)
        present = me >= distance
        level = jnp.where(present, level, -jnp.inf)
        decay = jnp.where(present, decay, 0.0)
        cut = jnp.where(present, cut, 0.0)
        term = dot_any(query_rows, memory, (((1,), (0,)), ((), ())))
        if earlier is None:
            earlier = (level, decay, cut)
            total = term
        else:
            level_later, decay_later, cut_later = earlier
            kept_level = jnp.where(cut_later > 0.5, -jnp.inf, level + decay_later)
            new_level = jnp.maximum(kept_level, level_later)
            safe_level = jnp.where(new_level == -jnp.inf, 0.0, new_level)
            total = jnp.exp(kept_level - safe_level) * term + jnp.exp(level_later - safe_level) * total
            earlier = (new_level, decay + decay_later, jnp.maximum(cut, cut_later))
        if 2 * distance < count:
            inclusive = combine((memory.astype(jnp.float32), level, decay, cut), inclusive)
        distance *= 2
    return total, earlier[0], local_parts


def body(token_ids, inner_x, out_gate, gate_pre, conv_weight, qkv_weight, norm_gain, skip_gain):
    num_rows, channels = inner_x.shape
    kernel_taps = conv_weight.shape[0]
    rim_rows = passed_along(inner_x[num_rows - kernel_taps + 1 :], AXES, 1)
    extended = jnp.concatenate([rim_rows, inner_x], axis=0)
    conv_sum = jnp.zeros((num_rows, channels), jnp.float32)
    for offset in range(kernel_taps):
        conv_sum = conv_sum + conv_weight[offset] * extended[offset : offset + num_rows].astype(
            jnp.float32
        )
    convolved = jax.nn.silu(conv_sum).astype(jnp.bfloat16)
    query_rows = jnp.dot(
        convolved, dense_blocks(qkv_weight[0], channels), preferred_element_type=jnp.float32
    ).astype(jnp.bfloat16)
    key_rows = (
        jnp.dot(
            convolved, dense_blocks(qkv_weight[1], channels), preferred_element_type=jnp.float32
        )
        * channels ** (-0.5)
    ).astype(jnp.bfloat16)
    value_rows = jnp.dot(
        inner_x, dense_blocks(qkv_weight[2], channels), preferred_element_type=jnp.float32
    ).astype(jnp.bfloat16)
    input_gate = gate_pre[0]
    log_decay = jnp.cumsum(jax.nn.log_sigmoid(gate_pre[1]))
    doc_marks = jnp.cumsum((token_ids == 0).astype(jnp.int32))
    last_mark = doc_marks[num_rows - 1]
    tail_weight = jnp.where(
        doc_marks == last_mark, log_decay[num_rows - 1] - log_decay + input_gate, -jnp.inf
    )
    tail_level = jnp.max(tail_weight)
    weighted_keys = jnp.exp(tail_weight - tail_level)[:, None] * key_rows.astype(jnp.float32)
    summary = dot_two_pass(weighted_keys, value_rows, (((0,), (0,)), ((), ())))
    own_state = (summary, tail_level, log_decay[num_rows - 1], (last_mark > 0).astype(jnp.float32))
    token_position = jnp.arange(num_rows)
    valid = (token_position[None, :] <= token_position[:, None]) & (
        doc_marks[None, :] == doc_marks[:, None]
    )
    log_weight = jnp.where(
        valid, log_decay[:, None] - log_decay[None, :] + input_gate[None, :], -jnp.inf
    )
    local_max = jnp.max(log_weight, axis=1)
    scores = lax.dot_general(
        query_rows, key_rows, (((1,), (1,)), ((), ())), preferred_element_type=jnp.float32
    )
    weights = jnp.exp(log_weight - local_max[:, None]) * scores
    local_sum = dot_two_pass(weights, value_rows, (((1,), (0,)), ((), ())))
    from_memory, incoming_level, (local_sum, local_max) = scan_and_read(
        own_state, lax.axis_index(AXES), lax.axis_size(AXES), query_rows, (local_sum, local_max)
    )
    carried = jnp.where(doc_marks == 0, log_decay + incoming_level, -jnp.inf)
    row_max = jnp.maximum(carried, local_max)
    retrieved = (
        jnp.exp(carried - row_max)[:, None] * from_memory
        + jnp.exp(local_max - row_max)[:, None] * local_sum
    )
    average = jnp.mean(retrieved, axis=1, keepdims=True)
    centered = retrieved - average
    variance = jnp.mean(centered * centered, axis=1, keepdims=True)
    normed = centered * lax.rsqrt(variance + 1e-05) * norm_gain
    gated_rows = (normed + skip_gain * convolved.astype(jnp.float32)) * jax.nn.silu(
        out_gate.astype(jnp.float32)
    )
    return gated_rows.astype(jnp.bfloat16)


def solution(mesh):
    return jax.shard_map(
        body,
        mesh=mesh,
        in_specs=(
            P(AXES),
            P(AXES, None),
            P(AXES, None),
            P(None, AXES),
            P(),
            P(),
            P(),
            P(),
        ),
        out_specs=P(AXES, None),
        check_vma=False,
    )
```
